128 devices in a mesh: prow: 8 (over x, core), pcol: 16 (over z, y).
Axes of the slice: x: 4, y: 4, z: 4, core: 2. Of those that a mesh axis runs over, the one named last changes fastest.
Arguments:
- front: float32 [16384, 16384], P('prow', 'pcol'), may hold values from -6 to 6
- fill_blocks: int32 [128, 128], P('prow', 'pcol'), may hold values from 0 to 1, as said below
- seg_values: float32 [262144, 128], P(('prow', 'pcol')), may hold values from -6 to 6
- seg_row: int32 [262144], P(('prow', 'pcol')), may hold values from 0 to 16383, as said below
- seg_block: int32 [262144], P(('prow', 'pcol')), may hold values from 0 to 127
- seg_live: int32 [128], P(('prow', 'pcol')), may hold values from 1024 to 2048, as said below
- panel_start: int32 [2], replicated, may hold values from 0 to 126, as said below
- panel_inverse: float32 [2, 256, 256], replicated
Outputs:
- factored: float32 [16384, 16384], P('prow', 'pcol')
The draws below stay inside these ranges and needn't reach their ends.
Inputs may be any that keep to these rules, and one draw needn't show every extreme that they name: `seg_row`: segments are ordered so that, among one device's live segments, at most 24 have rows in one block of F // 8 rows and column blocks in one group of 8 blocks; one such owner receives exactly 24 from every device. `seg_live`: some device has all its segments live. `fill_blocks`: Symmetric, with ones on the diagonal. `panel_start`: each is a multiple of 2; a panel lies within the columns of one index of pcol, and consecutive panels lie on different indices of pcol.
All inputs are finite; a program needn't handle non-finite values.
Results may differ from the reference program's by a relative error of at most 0.0001.
Values sent between devices are 32-bit elements; how exact they have to be, the bound alone decides.
No kernel may reach another device: no remote copies, remote signals or barrier semaphores. Data moves between devices by JAX's collectives and lax.ppermute only.
A program may use at most 128 MiB of HBM per device.

```python
import jax
import jax.numpy as jnp
from jax import lax

F = 16384
PW = 256
PANELS = 2
SEG_DEV = 2048
CAP = 24
SEGS = 262144
N_PROW = 8
N_PCOL = 16


def routes_common(key):
    devices = N_PROW * N_PCOL
    slots = devices * CAP
    rows_local = F // N_PROW
    blocks_local = F // 128 // N_PCOL
    keys = jax.random.split(jax.random.fold_in(key, 7), 5)
    bias = jax.random.randint(keys[0], (devices,), 0, 4)
    heavy = jax.random.randint(keys[1], (), 0, devices)
    bias = jnp.where(jnp.arange(devices) == heavy, 16, bias)
    slot_bias = jnp.repeat(bias, CAP)
    noise = jax.random.randint(keys[2], (devices, slots), 0, 4096)
    score = (noise + slot_bias[None, :] * 1024) * slots + jnp.arange(slots)[None, :]
    unused, chosen = lax.top_k(score, SEG_DEV)
    target = chosen // CAP
    row = target // N_PCOL * rows_local + jax.random.randint(keys[3], (devices, SEG_DEV), 0, rows_local)
    block = target % N_PCOL * blocks_local + jax.random.randint(keys[4], (devices, SEG_DEV), 0, blocks_local)
    return (row.reshape(-1).astype(jnp.int32), block.reshape(-1).astype(jnp.int32))


def draw_seg_row(key, part):
    return routes_common(key)[0]


def draw_seg_block(key, part):
    return routes_common(key)[1]


def draw_seg_live(key, part):
    devices = N_PROW * N_PCOL
    counts = jax.random.randint(jax.random.fold_in(key, 11), (devices,), SEG_DEV // 2, SEG_DEV + 1)
    fullest = jax.random.randint(jax.random.fold_in(key, 12), (), 0, devices)
    return jnp.where(jnp.arange(devices) == fullest, SEG_DEV, counts).astype(jnp.int32)


def draw_fill_blocks(key, part):
    blocks = F // 128
    level = jax.random.randint(jax.random.fold_in(key, 21), (blocks,), 1, 9)
    upper = jnp.triu(jax.random.randint(jax.random.fold_in(key, 22), (blocks, blocks), 0, 8))
    both = upper + jnp.triu(upper, 1).T
    limit = jnp.minimum(level[:, None], level[None, :])
    filled = (both < limit) | (jnp.arange(blocks)[:, None] == jnp.arange(blocks)[None, :])
    return filled.astype(jnp.int32)


def draw_panel_start(key, part):
    blocks_local = F // 128 // N_PCOL
    panel_blocks = PW // 128
    first = jax.random.randint(jax.random.fold_in(key, 31), (1,), 0, N_PCOL)
    offset = panel_blocks * jax.random.randint(jax.random.fold_in(key, 32), (PANELS,), 0, blocks_local // panel_blocks)
    steps = jax.random.randint(jax.random.fold_in(key, 33), (PANELS - 1,), 1, N_PCOL)
    owners = jnp.cumsum(jnp.concatenate([first, steps])) % N_PCOL
    owners = (owners + (N_PCOL - 1) - owners[PANELS - 1]) % N_PCOL
    last = jnp.arange(PANELS) == PANELS - 1
    offset = jnp.where(last, blocks_local - panel_blocks, offset)
    return (owners * blocks_local + offset).astype(jnp.int32)


def draw_panel_inverse(key, part):
    key_off = jax.random.fold_in(key, 41)
    key_diag = jax.random.fold_in(key, 42)
    off = jax.random.normal(key_off, (PANELS, PW, PW), jnp.float32) / PW
    diag = jax.random.uniform(key_diag, (PANELS, PW), jnp.float32, 0.04, 0.09)
    strict = jnp.triu(jnp.ones((PW, PW), jnp.float32), 1)
    eye = jnp.eye(PW, dtype=jnp.float32)
    return (off * strict[None] + diag[:, :, None] * eye[None]).astype(jnp.float32)


def block_scale(rng, extent, cuts, least, high):
    def one(dim, blocks):
        steps = jax.random.uniform(jax.random.fold_in(jax.random.fold_in(rng, 6), dim), (blocks,), jnp.float32, least / len(cuts), high / len(cuts))
        return jnp.repeat(jnp.exp(steps), extent[dim] // blocks).reshape((-1,) + (1,) * (len(extent) - dim - 1))

    level = one(*cuts[0])
    for cut in cuts[1:]:
        level = level * one(*cut)
    return level


def normal_values(own_key, dims, spread, most, cuts=(), kind=jnp.bfloat16):
    drawn = jax.random.normal(own_key, dims, jnp.float32) * spread
    if len(cuts) > 0:
        drawn = block_scale(own_key, dims, cuts, -0.22, 0.18) * drawn
    return jnp.clip(drawn, min=-most, max=most).astype(kind)


def setup_inputs(seed: int = 0) -> dict:
    splits = jax.random.split(jax.random.key(seed), 9)
    front = normal_values(splits[0], (F, F), 1.0, 6.0, ((0, 8), (1, 16)), jnp.float32)
    fill_blocks = draw_fill_blocks(jax.random.fold_in(splits[8], 71), 0)
    seg_values = normal_values(splits[2], (SEGS, 128), 1.0, 6.0, ((0, 128),), jnp.float32)
    seg_row = draw_seg_row(jax.random.fold_in(splits[8], 71), 0)
    seg_block = draw_seg_block(jax.random.fold_in(splits[8], 71), 0)
    seg_live = draw_seg_live(jax.random.fold_in(splits[8], 71), 0)
    panel_start = draw_panel_start(jax.random.fold_in(splits[8], 71), 0)
    panel_inverse = draw_panel_inverse(jax.random.fold_in(splits[8], 71), 0)
    return dict(front=front, fill_blocks=fill_blocks, seg_values=seg_values, seg_row=seg_row, seg_block=seg_block, seg_live=seg_live, panel_start=panel_start, panel_inverse=panel_inverse)


def apply_mask(product, fill_blocks):
    rows, cols = product.shape
    blocks = fill_blocks.astype(jnp.float32)
    shaped = product.reshape(rows // 128, 128, cols // 128, 128) * blocks[:, None, :, None]
    return shaped.reshape(rows, cols)


def reference(front, fill_blocks, seg_values, seg_row, seg_block, seg_live, panel_start, panel_inverse):
    n_seg = seg_values.shape[0]
    per_dev = n_seg // seg_live.shape[0]
    position = jnp.arange(n_seg, dtype=jnp.int32) % per_dev
    live = position < jnp.repeat(seg_live, per_dev)
    blocks = F // 128
    target = (seg_row * blocks + seg_block).astype(jnp.int32)
    added = jnp.where(live[:, None], seg_values, jnp.zeros_like(seg_values))
    flat = front.reshape(F * blocks, 128).at[target].add(added)
    current = flat.reshape(F, F)
    for k in range(PANELS):
        start = (panel_start[k] * 128).astype(jnp.int32)
        columns = lax.dynamic_slice_in_dim(current, start, PW, 1)
        left = jnp.dot(columns, panel_inverse[k], precision=lax.Precision.HIGHEST, preferred_element_type=jnp.float32)
        product = jnp.dot(left, left.T, precision=lax.Precision.HIGHEST, preferred_element_type=jnp.float32)
        current = current - apply_mask(product, fill_blocks)
    return current
```

```python
import jax
import jax.numpy as jnp
from jax import lax
from jax.sharding import PartitionSpec as P

PANELS = 2
HIGHEST = lax.Precision.HIGHEST


def dot(a, b):
    return jnp.dot(a, b, precision=HIGHEST, preferred_element_type=jnp.float32)


def dot_t(a, b):
    dims = (((1,), (1,)), ((), ()))
    return lax.dot_general(a, b, dims, precision=HIGHEST, preferred_element_type=jnp.float32)


def gather_rows(piece, axis, n):
    spread = jnp.broadcast_to(piece[None], (n,) + piece.shape)
    got = lax.all_to_all(spread, axis, 0, 0, tiled=False)
    return got.reshape(n * piece.shape[0], piece.shape[1])


def spread(x, total):
    for bit in range(total.bit_length() - 1):
        pairs = [(i, i ^ (1 << bit)) for i in range(total)]
        x = x + lax.ppermute(x, ("prow", "pcol"), pairs)
    return x


def assemble(front, seg_values, seg_row, seg_block, seg_live, n_prow, n_pcol):
    rows_local, cols_local = front.shape
    blocks_local = cols_local // 128
    devices = n_prow * n_pcol
    seg_count = seg_values.shape[0]
    capacity = 3 * seg_count // (2 * devices)
    target = seg_row // rows_local * n_pcol + seg_block // blocks_local
    live = jnp.arange(seg_count, dtype=jnp.int32) < seg_live[0]
    onehot = (target[:, None] == jnp.arange(devices, dtype=jnp.int32)[None, :]).astype(jnp.int32)
    earlier = jnp.cumsum(onehot, axis=0) - onehot
    rank = jnp.sum(earlier * onehot, axis=1)
    slot = jnp.where(live, target * capacity + rank, devices * capacity)
    local_place = (seg_row % rows_local * blocks_local + seg_block % blocks_local).astype(
        jnp.float32
    )
    send_values = (
        jnp.zeros((devices * capacity, 128), jnp.float32).at[slot].set(seg_values, mode="drop")
    )
    send_place = (
        jnp.zeros((devices * capacity,), jnp.float32).at[slot].set(local_place, mode="drop")
    )
    got_values = lax.all_to_all(send_values, ("prow", "pcol"), 0, 0, tiled=True)
    got_place = lax.all_to_all(send_place, ("prow", "pcol"), 0, 0, tiled=True)
    place = got_place.astype(jnp.int32)
    index = jnp.stack([place // blocks_local, place % blocks_local * 128], axis=1)
    numbers = lax.ScatterDimensionNumbers(
        update_window_dims=(1,), inserted_window_dims=(0,), scatter_dims_to_operand_dims=(0, 1)
    )
    return lax.scatter_add(front, index, got_values, numbers)


def body(front, fill_blocks, seg_values, seg_row, seg_block, seg_live, panel_start, panel_inverse):
    rows_local, cols_local = front.shape
    blocks_local = cols_local // 128
    n_prow = lax.axis_size("prow")
    n_pcol = lax.axis_size("pcol")
    pw = panel_inverse.shape[1]
    piece_rows = rows_local // n_pcol
    r = lax.axis_index("prow")
    c = lax.axis_index("pcol")

    mask_all = lax.all_gather(
        lax.all_gather(fill_blocks, "prow", axis=0, tiled=True), "pcol", axis=1, tiled=True
    ).astype(jnp.float32)

    assembled = assemble(front, seg_values, seg_row, seg_block, seg_live, n_prow, n_pcol)

    owner = [panel_start[k] // blocks_local for k in range(PANELS)]
    offset = [panel_start[k] % blocks_local * 128 for k in range(PANELS)]
    cols = [lax.dynamic_slice_in_dim(assembled, offset[k], pw, 1) for k in range(PANELS)]

    start2 = panel_start[1] * 128
    src_row = start2 // rows_local
    x_local = lax.dynamic_slice_in_dim(cols[0], start2 % rows_local, pw, 0)
    x_mine = jnp.where((r == src_row) & (c == owner[0]), x_local, 0.0)
    x_cols = spread(x_mine, n_prow * n_pcol)

    send = jnp.concatenate(cols, axis=1).reshape(n_pcol, piece_rows, PANELS * pw)
    recv = lax.all_to_all(send, "pcol", 0, 0, tiled=False)
    piece0 = lax.dynamic_index_in_dim(recv, owner[0], 0, keepdims=False)[:, :pw]
    piece1 = lax.dynamic_index_in_dim(recv, owner[1], 0, keepdims=False)[:, pw:]

    left0 = dot(piece0, panel_inverse[0])
    left0_x = dot(x_cols, panel_inverse[0])
    piece_block = (r * rows_local + c * piece_rows) // 128
    m_row = lax.dynamic_slice(mask_all, (piece_block, panel_start[1]), (1, pw // 128))
    m_piece = jnp.repeat(m_row, 128, axis=1)
    piece1 = piece1 - dot_t(left0, left0_x) * m_piece
    left1 = dot(piece1, panel_inverse[1])
    piece = jnp.concatenate([left0, left1], axis=1)

    left_rows = gather_rows(piece, "pcol", n_pcol)

    perm = []
    for sr in range(n_prow):
        for sc in range(n_pcol):
            first = sr * rows_local + sc * piece_rows
            dc = first // cols_local
            dr = first % cols_local // piece_rows
            perm.append((sr * n_pcol + sc, dr * n_pcol + dc))
    moved = lax.ppermute(piece, ("prow", "pcol"), perm)
    left_cols = gather_rows(moved, "prow", n_prow)

    product = dot_t(left_rows, left_cols)
    mask_local = fill_blocks.astype(jnp.float32)
    shaped = product.reshape(rows_local // 128, 128, blocks_local, 128) * mask_local[:, None, :, None]
    return assembled - shaped.reshape(rows_local, cols_local)


def solution(mesh):
    placed = (
        P("prow", "pcol"),
        P("prow", "pcol"),
        P(("prow", "pcol"), None),
        P(("prow", "pcol")),
        P(("prow", "pcol")),
        P(("prow", "pcol")),
        P(),
        P(),
    )
    return jax.shard_map(
        body, mesh=mesh, in_specs=placed, out_specs=P("prow", "pcol"), check_vma=False
    )
```

```python
import jax
import jax.numpy as jnp
from jax import lax
from jax.sharding import PartitionSpec as P

PANELS = 2
HIGHEST = lax.Precision.HIGHEST


def dot(a, b):
    return jnp.dot(a, b, precision=HIGHEST, preferred_element_type=jnp.float32)


def dot_t(a, b):
    dims = (((1,), (1,)), ((), ()))
    return lax.dot_general(a, b, dims, precision=HIGHEST, preferred_element_type=jnp.float32)


def gather_rows(piece, axis, n):
    spread = jnp.broadcast_to(piece[None], (n,) + piece.shape)
    got = lax.all_to_all(spread, axis, 0, 0, tiled=False)
    return got.reshape(n * piece.shape[0], piece.shape[1])


def spread(x, total):
    for bit in range(total.bit_length() - 1):
        pairs = [(i, i ^ (1 << bit)) for i in range(total)]
        x = x + lax.ppermute(x, ("prow", "pcol"), pairs)
    return x


def assemble(front, seg_values, seg_row, seg_block, seg_live, n_prow, n_pcol):
    rows_local, cols_local = front.shape
    blocks_local = cols_local // 128
    devices = n_prow * n_pcol
    seg_count = seg_values.shape[0]
    capacity = 3 * seg_count // (2 * devices)
    target = seg_row // rows_local * n_pcol + seg_block // blocks_local
    live = jnp.arange(seg_count, dtype=jnp.int32) < seg_live[0]
    onehot = (target[:, None] == jnp.arange(devices, dtype=jnp.int32)[None, :]).astype(jnp.int32)
    earlier = jnp.cumsum(onehot, axis=0) - onehot
    rank = jnp.sum(earlier * onehot, axis=1)
    slot = jnp.where(live, target * capacity + rank, devices * capacity)
    local_place = (seg_row % rows_local * blocks_local + seg_block % blocks_local).astype(
        jnp.float32
    )
    send_values = (
        jnp.zeros((devices * capacity, 128), jnp.float32).at[slot].set(seg_values, mode="drop")
    )
    send_place = (
        jnp.zeros((devices * capacity,), jnp.float32).at[slot].set(local_place, mode="drop")
    )
    got_values = lax.all_to_all(send_values, ("prow", "pcol"), 0, 0, tiled=True)
    got_place = lax.all_to_all(send_place, ("prow", "pcol"), 0, 0, tiled=True)
    flat = (
        front.reshape(rows_local * blocks_local, 128)
        .at[got_place.astype(jnp.int32)]
        .add(got_values)
    )
    return flat.reshape(rows_local, cols_local)


def body(front, fill_blocks, seg_values, seg_row, seg_block, seg_live, panel_start, panel_inverse):
    rows_local, cols_local = front.shape
    blocks_local = cols_local // 128
    n_prow = lax.axis_size("prow")
    n_pcol = lax.axis_size("pcol")
    pw = panel_inverse.shape[1]
    piece_rows = rows_local // n_pcol
    r = lax.axis_index("prow")
    c = lax.axis_index("pcol")

    mask_all = lax.all_gather(
        lax.all_gather(fill_blocks, "prow", axis=0, tiled=True), "pcol", axis=1, tiled=True
    ).astype(jnp.float32)

    assembled = assemble(front, seg_values, seg_row, seg_block, seg_live, n_prow, n_pcol)

    owner = [panel_start[k] // blocks_local for k in range(PANELS)]
    offset = [panel_start[k] % blocks_local * 128 for k in range(PANELS)]
    cols = [lax.dynamic_slice_in_dim(assembled, offset[k], pw, 1) for k in range(PANELS)]

    start2 = panel_start[1] * 128
    src_row = start2 // rows_local
    x_local = lax.dynamic_slice_in_dim(cols[0], start2 % rows_local, pw, 0)
    x_mine = jnp.where((r == src_row) & (c == owner[0]), x_local, 0.0)
    x_cols = spread(x_mine, n_prow * n_pcol)

    send = jnp.concatenate(cols, axis=1).reshape(n_pcol, piece_rows, PANELS * pw)
    recv = lax.all_to_all(send, "pcol", 0, 0, tiled=False)
    piece0 = lax.dynamic_index_in_dim(recv, owner[0], 0, keepdims=False)[:, :pw]
    piece1 = lax.dynamic_index_in_dim(recv, owner[1], 0, keepdims=False)[:, pw:]

    left0 = dot(piece0, panel_inverse[0])
    left0_x = dot(x_cols, panel_inverse[0])
    piece_block = (r * rows_local + c * piece_rows) // 128
    m_row = lax.dynamic_slice(mask_all, (piece_block, panel_start[1]), (1, pw // 128))
    m_piece = jnp.repeat(m_row, 128, axis=1)
    piece1 = piece1 - dot_t(left0, left0_x) * m_piece
    left1 = dot(piece1, panel_inverse[1])
    piece = jnp.concatenate([left0, left1], axis=1)

    left_rows = gather_rows(piece, "pcol", n_pcol)

    perm = []
    for sr in range(n_prow):
        for sc in range(n_pcol):
            first = sr * rows_local + sc * piece_rows
            dc = first // cols_local
            dr = first % cols_local // piece_rows
            perm.append((sr * n_pcol + sc, dr * n_pcol + dc))
    moved = lax.ppermute(piece, ("prow", "pcol"), perm)
    left_cols = gather_rows(moved, "prow", n_prow)

    product = dot_t(left_rows, left_cols)
    mask_local = fill_blocks.astype(jnp.float32)
    shaped = product.reshape(rows_local // 128, 128, blocks_local, 128) * mask_local[:, None, :, None]
    return assembled - shaped.reshape(rows_local, cols_local)


def solution(mesh):
    placed = (
        P("prow", "pcol"),
        P("prow", "pcol"),
        P(("prow", "pcol"), None),
        P(("prow", "pcol")),
        P(("prow", "pcol")),
        P(("prow", "pcol")),
        P(),
        P(),
    )
    return jax.shard_map(
        body, mesh=mesh, in_specs=placed, out_specs=P("prow", "pcol"), check_vma=False
    )
```

```python
import jax
import jax.numpy as jnp
from jax import lax
from jax.sharding import PartitionSpec as P

PANELS = 2
HIGHEST = lax.Precision.HIGHEST


def dot(a, b):
    return jnp.dot(a, b, precision=HIGHEST, preferred_element_type=jnp.float32)


def dot_t(a, b):
    dims = (((1,), (1,)), ((), ()))
    return lax.dot_general(a, b, dims, precision=HIGHEST, preferred_element_type=jnp.float32)


def gather_rows(piece, axis, n):
    spread = jnp.broadcast_to(piece[None], (n,) + piece.shape)
    got = lax.all_to_all(spread, axis, 0, 0, tiled=False)
    return got.reshape(n * piece.shape[0], piece.shape[1])


def spread(x, total):
    for bit in range(total.bit_length() - 1):
        pairs = [(i, i ^ (1 << bit)) for i in range(total)]
        x = x + lax.ppermute(x, ("prow", "pcol"), pairs)
    return x


def assemble(front, seg_values, seg_row, seg_block, seg_live, n_prow, n_pcol):
    rows_local, cols_local = front.shape
    blocks_local = cols_local // 128
    devices = n_prow * n_pcol
    seg_count = seg_values.shape[0]
    capacity = 3 * seg_count // (2 * devices)
    target = seg_row // rows_local * n_pcol + seg_block // blocks_local
    live = jnp.arange(seg_count, dtype=jnp.int32) < seg_live[0]
    onehot = (target[:, None] == jnp.arange(devices, dtype=jnp.int32)[None, :]).astype(jnp.int32)
    earlier = jnp.cumsum(onehot, axis=0) - onehot
    rank = jnp.sum(earlier * onehot, axis=1)
    slot = jnp.where(live, target * capacity + rank, devices * capacity)
    local_place = (seg_row % rows_local * blocks_local + seg_block % blocks_local).astype(
        jnp.float32
    )
    send_values = (
        jnp.zeros((devices * capacity, 128), jnp.float32).at[slot].set(seg_values, mode="drop")
    )
    send_place = (
        jnp.zeros((devices * capacity,), jnp.float32).at[slot].set(local_place, mode="drop")
    )
    got_values = lax.all_to_all(send_values, ("prow", "pcol"), 0, 0, tiled=True)
    got_place = lax.all_to_all(send_place, ("prow", "pcol"), 0, 0, tiled=True)
    flat = (
        front.reshape(rows_local * blocks_local, 128)
        .at[got_place.astype(jnp.int32)]
        .add(got_values)
    )
    return flat.reshape(rows_local, cols_local)


def body(front, fill_blocks, seg_values, seg_row, seg_block, seg_live, panel_start, panel_inverse):
    rows_local, cols_local = front.shape
    blocks_local = cols_local // 128
    n_prow = lax.axis_size("prow")
    n_pcol = lax.axis_size("pcol")
    pw = panel_inverse.shape[1]
    piece_rows = rows_local // n_pcol
    r = lax.axis_index("prow")
    c = lax.axis_index("pcol")

    assembled = assemble(front, seg_values, seg_row, seg_block, seg_live, n_prow, n_pcol)

    owner = [panel_start[k] // blocks_local for k in range(PANELS)]
    offset = [panel_start[k] % blocks_local * 128 for k in range(PANELS)]
    cols = [lax.dynamic_slice_in_dim(assembled, offset[k], pw, 1) for k in range(PANELS)]

    start2 = panel_start[1] * 128
    src_row = start2 // rows_local
    x_local = lax.dynamic_slice_in_dim(cols[0], start2 % rows_local, pw, 0)
    x_mine = jnp.where((r == src_row) & (c == owner[0]), x_local, 0.0)
    x_cols = spread(x_mine, n_prow * n_pcol)

    mask_local = fill_blocks.astype(jnp.float32)
    mask_two = lax.dynamic_slice_in_dim(mask_local, offset[1] // 128, pw // 128, 1)
    mask_two = jnp.repeat(mask_two.reshape(n_pcol, piece_rows // 128, pw // 128), 128, axis=2)
    mask_two = jnp.pad(mask_two.reshape(n_pcol, 1, pw), ((0, 0), (0, 0), (0, (PANELS - 1) * pw)))
    send = jnp.concatenate(cols, axis=1).reshape(n_pcol, piece_rows, PANELS * pw)
    send = jnp.concatenate([send, mask_two], axis=1)
    recv = lax.all_to_all(send, "pcol", 0, 0, tiled=False)
    piece0 = lax.dynamic_index_in_dim(recv, owner[0], 0, keepdims=False)[:piece_rows, :pw]
    from_two = lax.dynamic_index_in_dim(recv, owner[1], 0, keepdims=False)
    piece1 = from_two[:piece_rows, pw:]
    m_piece = from_two[piece_rows:, :pw]

    left0 = dot(piece0, panel_inverse[0])
    left0_x = dot(x_cols, panel_inverse[0])
    piece1 = piece1 - dot_t(left0, left0_x) * m_piece
    left1 = dot(piece1, panel_inverse[1])
    piece = jnp.concatenate([left0, left1], axis=1)

    left_rows = gather_rows(piece, "pcol", n_pcol)

    perm = []
    for sr in range(n_prow):
        for sc in range(n_pcol):
            first = sr * rows_local + sc * piece_rows
            dc = first // cols_local
            dr = first % cols_local // piece_rows
            perm.append((sr * n_pcol + sc, dr * n_pcol + dc))
    moved = lax.ppermute(piece, ("prow", "pcol"), perm)
    left_cols = lax.all_gather(moved, "prow", axis=0, tiled=True)

    product = dot(left_rows, left_cols.T)
    shaped = product.reshape(rows_local // 128, 128, blocks_local, 128) * mask_local[:, None, :, None]
    return assembled - shaped.reshape(rows_local, cols_local)


def solution(mesh):
    placed = (
        P("prow", "pcol"),
        P("prow", "pcol"),
        P(("prow", "pcol"), None),
        P(("prow", "pcol")),
        P(("prow", "pcol")),
        P(("prow", "pcol")),
        P(),
        P(),
    )
    return jax.shard_map(
        body, mesh=mesh, in_specs=placed, out_specs=P("prow", "pcol"), check_vma=False
    )
```

```python
import jax
import jax.numpy as jnp
from jax import lax
from jax.sharding import PartitionSpec as P

PANELS = 2
HIGHEST = lax.Precision.HIGHEST


def dot(a, b):
    return jnp.dot(a, b, precision=HIGHEST, preferred_element_type=jnp.float32)


def dot_t(a, b):
    dims = (((1,), (1,)), ((), ()))
    return lax.dot_general(a, b, dims, precision=HIGHEST, preferred_element_type=jnp.float32)


def gather_rows(piece, axis, n):
    spread = jnp.broadcast_to(piece[None], (n,) + piece.shape)
    got = lax.all_to_all(spread, axis, 0, 0, tiled=False)
    return got.reshape(n * piece.shape[0], piece.shape[1])


def spread(x, total):
    for bit in range(total.bit_length() - 1):
        pairs = [(i, i ^ (1 << bit)) for i in range(total)]
        x = x + lax.ppermute(x, ("prow", "pcol"), pairs)
    return x


def assemble(front, seg_values, seg_row, seg_block, seg_live, n_prow, n_pcol):
    rows_local, cols_local = front.shape
    blocks_local = cols_local // 128
    devices = n_prow * n_pcol
    seg_count = seg_values.shape[0]
    capacity = 3 * seg_count // (2 * devices)
    target = seg_row // rows_local * n_pcol + seg_block // blocks_local
    live = jnp.arange(seg_count, dtype=jnp.int32) < seg_live[0]
    onehot = (target[:, None] == jnp.arange(devices, dtype=jnp.int32)[None, :]).astype(jnp.int32)
    earlier = jnp.cumsum(onehot, axis=0) - onehot
    rank = jnp.sum(earlier * onehot, axis=1)
    slot = jnp.where(live, target * capacity + rank, devices * capacity)
    local_place = (seg_row % rows_local * blocks_local + seg_block % blocks_local).astype(
        jnp.float32
    )
    send_values = (
        jnp.zeros((devices * capacity, 128), jnp.float32).at[slot].set(seg_values, mode="drop")
    )
    send_place = (
        jnp.zeros((devices * capacity,), jnp.float32).at[slot].set(local_place, mode="drop")
    )
    got_values = lax.all_to_all(send_values, ("prow", "pcol"), 0, 0, tiled=True)
    got_place = lax.all_to_all(send_place, ("prow", "pcol"), 0, 0, tiled=True)
    flat = (
        front.reshape(rows_local * blocks_local, 128)
        .at[got_place.astype(jnp.int32)]
        .add(got_values)
    )
    return flat.reshape(rows_local, cols_local)


def body(front, fill_blocks, seg_values, seg_row, seg_block, seg_live, panel_start, panel_inverse):
    rows_local, cols_local = front.shape
    blocks_local = cols_local // 128
    n_prow = lax.axis_size("prow")
    n_pcol = lax.axis_size("pcol")
    pw = panel_inverse.shape[1]
    piece_rows = rows_local // n_pcol
    r = lax.axis_index("prow")
    c = lax.axis_index("pcol")

    assembled = assemble(front, seg_values, seg_row, seg_block, seg_live, n_prow, n_pcol)

    owner = [panel_start[k] // blocks_local for k in range(PANELS)]
    offset = [panel_start[k] % blocks_local * 128 for k in range(PANELS)]
    cols = [lax.dynamic_slice_in_dim(assembled, offset[k], pw, 1) for k in range(PANELS)]

    start2 = panel_start[1] * 128
    src_row = start2 // rows_local
    x_local = lax.dynamic_slice_in_dim(cols[0], start2 % rows_local, pw, 0)
    x_mine = jnp.where((r == src_row) & (c == owner[0]), x_local, 0.0)
    x_cols = spread(x_mine, n_prow * n_pcol)

    mask_local = fill_blocks.astype(jnp.float32)
    mask_two = lax.dynamic_slice_in_dim(mask_local, offset[1] // 128, pw // 128, 1)
    mask_two = jnp.repeat(mask_two.reshape(n_pcol, piece_rows // 128, pw // 128), 128, axis=2)
    mask_two = jnp.pad(mask_two.reshape(n_pcol, 1, pw), ((0, 0), (0, 0), (0, (PANELS - 1) * pw)))
    send = jnp.concatenate(cols, axis=1).reshape(n_pcol, piece_rows, PANELS * pw)
    send = jnp.concatenate([send, mask_two], axis=1)
    recv = lax.all_to_all(send, "pcol", 0, 0, tiled=False)
    piece0 = lax.dynamic_index_in_dim(recv, owner[0], 0, keepdims=False)[:piece_rows, :pw]
    from_two = lax.dynamic_index_in_dim(recv, owner[1], 0, keepdims=False)
    piece1 = from_two[:piece_rows, pw:]
    m_piece = from_two[piece_rows:, :pw]

    left0 = dot(piece0, panel_inverse[0])
    left0_x = dot(x_cols, panel_inverse[0])
    piece1 = piece1 - dot_t(left0, left0_x) * m_piece
    left1 = dot(piece1, panel_inverse[1])
    piece = jnp.concatenate([left0, left1], axis=1)

    left_rows = gather_rows(piece, "pcol", n_pcol)

    perm = []
    for sr in range(n_prow):
        for sc in range(n_pcol):
            first = sr * rows_local + sc * piece_rows
            dc = first // cols_local
            dr = first % cols_local // piece_rows
            perm.append((sr * n_pcol + sc, dr * n_pcol + dc))
    moved = lax.ppermute(piece, ("prow", "pcol"), perm)
    left_cols = lax.all_gather(moved, "prow", axis=0, tiled=True)

    product = dot(left_rows, left_cols.T)
    mask_full = jnp.repeat(jnp.repeat(mask_local, 128, axis=0), 128, axis=1)
    return assembled - product * mask_full


def solution(mesh):
    placed = (
        P("prow", "pcol"),
        P("prow", "pcol"),
        P(("prow", "pcol"), None),
        P(("prow", "pcol")),
        P(("prow", "pcol")),
        P(("prow", "pcol")),
        P(),
        P(),
    )
    return jax.shard_map(
        body, mesh=mesh, in_specs=placed, out_specs=P("prow", "pcol"), check_vma=False
    )
```

```python
import jax
import jax.numpy as jnp
from jax import lax
from jax.sharding import PartitionSpec as P

PANELS = 2
HIGHEST = lax.Precision.HIGHEST


def dot(a, b):
    return jnp.dot(a, b, precision=HIGHEST, preferred_element_type=jnp.float32)


def dot_t(a, b):
    dims = (((1,), (1,)), ((), ()))
    return lax.dot_general(a, b, dims, precision=HIGHEST, preferred_element_type=jnp.float32)


def gather_rows(piece, axis, n):
    spread = jnp.broadcast_to(piece[None], (n,) + piece.shape)
    got = lax.all_to_all(spread, axis, 0, 0, tiled=False)
    return got.reshape(n * piece.shape[0], piece.shape[1])


def spread(x, total):
    for bit in range(total.bit_length() - 1):
        pairs = [(i, i ^ (1 << bit)) for i in range(total)]
        x = x + lax.ppermute(x, ("prow", "pcol"), pairs)
    return x


def assemble(front, seg_values, seg_row, seg_block, seg_live, n_prow, n_pcol):
    rows_local, cols_local = front.shape
    blocks_local = cols_local // 128
    devices = n_prow * n_pcol
    seg_count = seg_values.shape[0]
    capacity = 3 * seg_count // (2 * devices)
    target = seg_row // rows_local * n_pcol + seg_block // blocks_local
    live = jnp.arange(seg_count, dtype=jnp.int32) < seg_live[0]
    onehot = (target[:, None] == jnp.arange(devices, dtype=jnp.int32)[None, :]).astype(jnp.int32)
    earlier = jnp.cumsum(onehot, axis=0) - onehot
    rank = jnp.sum(earlier * onehot, axis=1)
    slot = jnp.where(live, target * capacity + rank, devices * capacity)
    local_place = (seg_row % rows_local * blocks_local + seg_block % blocks_local).astype(
        jnp.float32
    )
    send_values = (
        jnp.zeros((devices * capacity, 128), jnp.float32).at[slot].set(seg_values, mode="drop")
    )
    send_place = (
        jnp.zeros((devices * capacity,), jnp.float32).at[slot].set(local_place, mode="drop")
    )
    got_values = lax.all_to_all(send_values, ("prow", "pcol"), 0, 0, tiled=True)
    got_place = lax.all_to_all(send_place, ("prow", "pcol"), 0, 0, tiled=True)
    flat = (
        front.reshape(rows_local * blocks_local, 128)
        .at[got_place.astype(jnp.int32)]
        .add(got_values)
    )
    return flat.reshape(rows_local, cols_local)


def body(front, fill_blocks, seg_values, seg_row, seg_block, seg_live, panel_start, panel_inverse):
    rows_local, cols_local = front.shape
    blocks_local = cols_local // 128
    n_prow = lax.axis_size("prow")
    n_pcol = lax.axis_size("pcol")
    pw = panel_inverse.shape[1]
    piece_rows = rows_local // n_pcol
    r = lax.axis_index("prow")
    c = lax.axis_index("pcol")

    assembled = assemble(front, seg_values, seg_row, seg_block, seg_live, n_prow, n_pcol)

    owner = [panel_start[k] // blocks_local for k in range(PANELS)]
    offset = [panel_start[k] % blocks_local * 128 for k in range(PANELS)]
    cols = [lax.dynamic_slice_in_dim(assembled, offset[k], pw, 1) for k in range(PANELS)]

    start2 = panel_start[1] * 128
    src_row = start2 // rows_local
    x_local = lax.dynamic_slice_in_dim(cols[0], start2 % rows_local, pw, 0)
    x_mine = jnp.where((r == src_row) & (c == owner[0]), x_local, 0.0)
    x_cols = lax.psum(lax.psum(x_mine, "pcol"), "prow")

    mask_local = fill_blocks.astype(jnp.float32)
    mask_two = lax.dynamic_slice_in_dim(mask_local, offset[1] // 128, pw // 128, 1)
    mask_two = jnp.repeat(mask_two.reshape(n_pcol, piece_rows // 128, pw // 128), 128, axis=2)
    mask_two = jnp.pad(mask_two.reshape(n_pcol, 1, pw), ((0, 0), (0, 0), (0, (PANELS - 1) * pw)))
    send = jnp.concatenate(cols, axis=1).reshape(n_pcol, piece_rows, PANELS * pw)
    send = jnp.concatenate([send, mask_two], axis=1)
    recv = lax.all_to_all(send, "pcol", 0, 0, tiled=False)
    piece0 = lax.dynamic_index_in_dim(recv, owner[0], 0, keepdims=False)[:piece_rows, :pw]
    from_two = lax.dynamic_index_in_dim(recv, owner[1], 0, keepdims=False)
    piece1 = from_two[:piece_rows, pw:]
    m_piece = from_two[piece_rows:, :pw]

    left0 = dot(piece0, panel_inverse[0])
    left0_x = dot(x_cols, panel_inverse[0])
    piece1 = piece1 - dot_t(left0, left0_x) * m_piece
    left1 = dot(piece1, panel_inverse[1])
    piece = jnp.concatenate([left0, left1], axis=1)

    left_rows = gather_rows(piece, "pcol", n_pcol)

    perm = []
    for sr in range(n_prow):
        for sc in range(n_pcol):
            first = sr * rows_local + sc * piece_rows
            dc = first // cols_local
            dr = first % cols_local // piece_rows
            perm.append((sr * n_pcol + sc, dr * n_pcol + dc))
    moved = lax.ppermute(piece, ("prow", "pcol"), perm)
    left_cols = lax.all_gather(moved, "prow", axis=0, tiled=True)

    product = jnp.dot(
        left_rows, left_cols.T, precision=lax.Precision.HIGH, preferred_element_type=jnp.float32
    )
    mask_full = jnp.repeat(jnp.repeat(mask_local, 128, axis=0), 128, axis=1)
    return assembled - product * mask_full


def solution(mesh):
    placed = (
        P("prow", "pcol"),
        P("prow", "pcol"),
        P(("prow", "pcol"), None),
        P(("prow", "pcol")),
        P(("prow", "pcol")),
        P(("prow", "pcol")),
        P(),
        P(),
    )
    return jax.shard_map(
        body, mesh=mesh, in_specs=placed, out_specs=P("prow", "pcol"), check_vma=False
    )
```

```python
import jax
import jax.numpy as jnp
from jax import lax
from jax.sharding import PartitionSpec as P

PANELS = 2
HIGHEST = lax.Precision.HIGHEST


def dot(a, b):
    return jnp.dot(a, b, precision=HIGHEST, preferred_element_type=jnp.float32)


def dot_t(a, b):
    dims = (((1,), (1,)), ((), ()))
    return lax.dot_general(a, b, dims, precision=HIGHEST, preferred_element_type=jnp.float32)


def gather_rows(piece, axis, n):
    spread = jnp.broadcast_to(piece[None], (n,) + piece.shape)
    got = lax.all_to_all(spread, axis, 0, 0, tiled=False)
    return got.reshape(n * piece.shape[0], piece.shape[1])


def spread(x, total):
    for bit in range(total.bit_length() - 1):
        pairs = [(i, i ^ (1 << bit)) for i in range(total)]
        x = x + lax.ppermute(x, ("prow", "pcol"), pairs)
    return x


def assemble(front, seg_values, seg_row, seg_block, seg_live, n_prow, n_pcol):
    rows_local, cols_local = front.shape
    blocks_local = cols_local // 128
    devices = n_prow * n_pcol
    seg_count = seg_values.shape[0]
    capacity = 3 * seg_count // (2 * devices)
    target = seg_row // rows_local * n_pcol + seg_block // blocks_local
    live = jnp.arange(seg_count, dtype=jnp.int32) < seg_live[0]
    onehot = (target[:, None] == jnp.arange(devices, dtype=jnp.int32)[None, :]).astype(jnp.int32)
    earlier = jnp.cumsum(onehot, axis=0) - onehot
    rank = jnp.sum(earlier * onehot, axis=1)
    slot = jnp.where(live, target * capacity + rank, devices * capacity)
    local_place = (seg_row % rows_local * blocks_local + seg_block % blocks_local).astype(
        jnp.float32
    )
    send_values = (
        jnp.zeros((devices * capacity, 128), jnp.float32).at[slot].set(seg_values, mode="drop")
    )
    send_place = (
        jnp.zeros((devices * capacity,), jnp.float32).at[slot].set(local_place, mode="drop")
    )
    got_values = lax.all_to_all(send_values, ("prow", "pcol"), 0, 0, tiled=True)
    got_place = lax.all_to_all(send_place, ("prow", "pcol"), 0, 0, tiled=True)
    flat = (
        front.reshape(rows_local * blocks_local, 128)
        .at[got_place.astype(jnp.int32)]
        .add(got_values)
    )
    return flat.reshape(rows_local, cols_local)


def body(front, fill_blocks, seg_values, seg_row, seg_block, seg_live, panel_start, panel_inverse):
    rows_local, cols_local = front.shape
    blocks_local = cols_local // 128
    n_prow = lax.axis_size("prow")
    n_pcol = lax.axis_size("pcol")
    pw = panel_inverse.shape[1]
    piece_rows = rows_local // n_pcol
    r = lax.axis_index("prow")
    c = lax.axis_index("pcol")

    assembled = assemble(front, seg_values, seg_row, seg_block, seg_live, n_prow, n_pcol)

    owner = [panel_start[k] // blocks_local for k in range(PANELS)]
    offset = [panel_start[k] % blocks_local * 128 for k in range(PANELS)]
    cols = [lax.dynamic_slice_in_dim(assembled, offset[k], pw, 1) for k in range(PANELS)]

    start2 = panel_start[1] * 128
    src_row = start2 // rows_local
    x_local = lax.dynamic_slice_in_dim(cols[0], start2 % rows_local, pw, 0)
    x_mine = jnp.where((r == src_row) & (c == owner[0]), x_local, 0.0)
    x_cols = spread(x_mine, n_prow * n_pcol)

    mask_local = fill_blocks.astype(jnp.float32)
    mask_two = lax.dynamic_slice_in_dim(mask_local, offset[1] // 128, pw // 128, 1)
    mask_two = jnp.repeat(mask_two.reshape(n_pcol, piece_rows // 128, pw // 128), 128, axis=2)
    mask_two = jnp.pad(mask_two.reshape(n_pcol, 1, pw), ((0, 0), (0, 0), (0, (PANELS - 1) * pw)))
    send = jnp.concatenate(cols, axis=1).reshape(n_pcol, piece_rows, PANELS * pw)
    send = jnp.concatenate([send, mask_two], axis=1)
    recv = lax.all_to_all(send, "pcol", 0, 0, tiled=False)
    piece0 = lax.dynamic_index_in_dim(recv, owner[0], 0, keepdims=False)[:piece_rows, :pw]
    from_two = lax.dynamic_index_in_dim(recv, owner[1], 0, keepdims=False)
    piece1 = from_two[:piece_rows, pw:]
    m_piece = from_two[piece_rows:, :pw]

    left0 = dot(piece0, panel_inverse[0])
    left0_x = dot(x_cols, panel_inverse[0])
    piece1 = piece1 - dot_t(left0, left0_x) * m_piece
    left1 = dot(piece1, panel_inverse[1])
    piece = jnp.concatenate([left0, left1], axis=1)

    left_rows = gather_rows(piece, "pcol", n_pcol)

    perm = []
    for sr in range(n_prow):
        for sc in range(n_pcol):
            first = sr * rows_local + sc * piece_rows
            dc = first // cols_local
            dr = first % cols_local // piece_rows
            perm.append((sr * n_pcol + sc, dr * n_pcol + dc))
    moved = lax.ppermute(piece, ("prow", "pcol"), perm)
    left_cols = lax.all_gather(moved, "prow", axis=0, tiled=True)

    product = jnp.dot(
        left_rows, left_cols.T, precision=lax.Precision.HIGH, preferred_element_type=jnp.float32
    )
    mask_full = jnp.repeat(jnp.repeat(mask_local, 128, axis=0), 128, axis=1)
    return assembled - product * mask_full


def solution(mesh):
    placed = (
        P("prow", "pcol"),
        P("prow", "pcol"),
        P(("prow", "pcol"), None),
        P(("prow", "pcol")),
        P(("prow", "pcol")),
        P(("prow", "pcol")),
        P(),
        P(),
    )
    return jax.shard_map(
        body, mesh=mesh, in_specs=placed, out_specs=P("prow", "pcol"), check_vma=False
    )
```

```python
import jax
import jax.numpy as jnp
from jax import lax
from jax.sharding import PartitionSpec as P

PANELS = 2
HIGHEST = lax.Precision.HIGHEST


def dot(a, b):
    return jnp.dot(a, b, precision=HIGHEST, preferred_element_type=jnp.float32)


def dot_t(a, b):
    dims = (((1,), (1,)), ((), ()))
    return lax.dot_general(a, b, dims, precision=HIGHEST, preferred_element_type=jnp.float32)


def gather_rows(piece, axis, n):
    spread = jnp.broadcast_to(piece[None], (n,) + piece.shape)
    got = lax.all_to_all(spread, axis, 0, 0, tiled=False)
    return got.reshape(n * piece.shape[0], piece.shape[1])


def spread(x, total):
    bits = total.bit_length() - 1
    low = 0
    while low < bits:
        width = min(2, bits - low)
        got = []
        for k in range(1, 1 << width):
            pairs = [(i, i ^ (k << low)) for i in range(total)]
            got.append(lax.ppermute(x, ("prow", "pcol"), pairs))
        for part in got:
            x = x + part
        low += width
    return x


def assemble(front, seg_values, seg_row, seg_block, seg_live, n_prow, n_pcol):
    rows_local, cols_local = front.shape
    blocks_local = cols_local // 128
    devices = n_prow * n_pcol
    seg_count = seg_values.shape[0]
    capacity = 3 * seg_count // (2 * devices)
    target = seg_row // rows_local * n_pcol + seg_block // blocks_local
    live = jnp.arange(seg_count, dtype=jnp.int32) < seg_live[0]
    onehot = (target[:, None] == jnp.arange(devices, dtype=jnp.int32)[None, :]).astype(jnp.int32)
    earlier = jnp.cumsum(onehot, axis=0) - onehot
    rank = jnp.sum(earlier * onehot, axis=1)
    slot = jnp.where(live, target * capacity + rank, devices * capacity)
    local_place = (seg_row % rows_local * blocks_local + seg_block % blocks_local).astype(
        jnp.float32
    )
    send_values = (
        jnp.zeros((devices * capacity, 128), jnp.float32).at[slot].set(seg_values, mode="drop")
    )
    send_place = (
        jnp.zeros((devices * capacity,), jnp.float32).at[slot].set(local_place, mode="drop")
    )
    got_values = lax.all_to_all(send_values, ("prow", "pcol"), 0, 0, tiled=True)
    got_place = lax.all_to_all(send_place, ("prow", "pcol"), 0, 0, tiled=True)
    flat = (
        front.reshape(rows_local * blocks_local, 128)
        .at[got_place.astype(jnp.int32)]
        .add(got_values)
    )
    return flat.reshape(rows_local, cols_local)


def body(front, fill_blocks, seg_values, seg_row, seg_block, seg_live, panel_start, panel_inverse):
    rows_local, cols_local = front.shape
    blocks_local = cols_local // 128
    n_prow = lax.axis_size("prow")
    n_pcol = lax.axis_size("pcol")
    pw = panel_inverse.shape[1]
    piece_rows = rows_local // n_pcol
    r = lax.axis_index("prow")
    c = lax.axis_index("pcol")

    assembled = assemble(front, seg_values, seg_row, seg_block, seg_live, n_prow, n_pcol)

    owner = [panel_start[k] // blocks_local for k in range(PANELS)]
    offset = [panel_start[k] % blocks_local * 128 for k in range(PANELS)]
    cols = [lax.dynamic_slice_in_dim(assembled, offset[k], pw, 1) for k in range(PANELS)]

    start2 = panel_start[1] * 128
    src_row = start2 // rows_local
    x_local = lax.dynamic_slice_in_dim(cols[0], start2 % rows_local, pw, 0)
    x_mine = jnp.where((r == src_row) & (c == owner[0]), x_local, 0.0)
    x_cols = spread(x_mine, n_prow * n_pcol)

    mask_local = fill_blocks.astype(jnp.float32)
    mask_two = lax.dynamic_slice_in_dim(mask_local, offset[1] // 128, pw // 128, 1)
    mask_two = jnp.repeat(mask_two.reshape(n_pcol, piece_rows // 128, pw // 128), 128, axis=2)
    mask_two = jnp.pad(mask_two.reshape(n_pcol, 1, pw), ((0, 0), (0, 0), (0, (PANELS - 1) * pw)))
    send = jnp.concatenate(cols, axis=1).reshape(n_pcol, piece_rows, PANELS * pw)
    send = jnp.concatenate([send, mask_two], axis=1)
    recv = lax.all_to_all(send, "pcol", 0, 0, tiled=False)
    piece0 = lax.dynamic_index_in_dim(recv, owner[0], 0, keepdims=False)[:piece_rows, :pw]
    from_two = lax.dynamic_index_in_dim(recv, owner[1], 0, keepdims=False)
    piece1 = from_two[:piece_rows, pw:]
    m_piece = from_two[piece_rows:, :pw]

    left0 = dot(piece0, panel_inverse[0])
    left0_x = dot(x_cols, panel_inverse[0])
    piece1 = piece1 - dot_t(left0, left0_x) * m_piece
    left1 = dot(piece1, panel_inverse[1])
    piece = jnp.concatenate([left0, left1], axis=1)

    left_rows = gather_rows(piece, "pcol", n_pcol)

    perm = []
    for sr in range(n_prow):
        for sc in range(n_pcol):
            first = sr * rows_local + sc * piece_rows
            dc = first // cols_local
            dr = first % cols_local // piece_rows
            perm.append((sr * n_pcol + sc, dr * n_pcol + dc))
    moved = lax.ppermute(piece, ("prow", "pcol"), perm)
    left_cols = lax.all_gather(moved, "prow", axis=0, tiled=True)

    product = jnp.dot(
        left_rows, left_cols.T, precision=lax.Precision.HIGH, preferred_element_type=jnp.float32
    )
    mask_full = jnp.repeat(jnp.repeat(mask_local, 128, axis=0), 128, axis=1)
    return assembled - product * mask_full


def solution(mesh):
    placed = (
        P("prow", "pcol"),
        P("prow", "pcol"),
        P(("prow", "pcol"), None),
        P(("prow", "pcol")),
        P(("prow", "pcol")),
        P(("prow", "pcol")),
        P(),
        P(),
    )
    return jax.shard_map(
        body, mesh=mesh, in_specs=placed, out_specs=P("prow", "pcol"), check_vma=False
    )
```

```python
import jax
import jax.numpy as jnp
from jax import lax
from jax.sharding import PartitionSpec as P

PANELS = 2
HIGHEST = lax.Precision.HIGHEST


def dot(a, b):
    return jnp.dot(a, b, precision=HIGHEST, preferred_element_type=jnp.float32)


def dot_t(a, b):
    dims = (((1,), (1,)), ((), ()))
    return lax.dot_general(a, b, dims, precision=HIGHEST, preferred_element_type=jnp.float32)


def gather_rows(piece, axis, n):
    spread = jnp.broadcast_to(piece[None], (n,) + piece.shape)
    got = lax.all_to_all(spread, axis, 0, 0, tiled=False)
    return got.reshape(n * piece.shape[0], piece.shape[1])


def spread(x, total):
    for bit in range(total.bit_length() - 1):
        pairs = [(i, i ^ (1 << bit)) for i in range(total)]
        x = x + lax.ppermute(x, ("prow", "pcol"), pairs)
    return x


def assemble(front, seg_values, seg_row, seg_block, seg_live, n_prow, n_pcol):
    rows_local, cols_local = front.shape
    blocks_local = cols_local // 128
    devices = n_prow * n_pcol
    seg_count = seg_values.shape[0]
    capacity = 3 * seg_count // (2 * devices)
    target = seg_row // rows_local * n_pcol + seg_block // blocks_local
    live = jnp.arange(seg_count, dtype=jnp.int32) < seg_live[0]
    onehot = (target[:, None] == jnp.arange(devices, dtype=jnp.int32)[None, :]).astype(jnp.int32)
    earlier = jnp.cumsum(onehot, axis=0) - onehot
    rank = jnp.sum(earlier * onehot, axis=1)
    slot = jnp.where(live, target * capacity + rank, devices * capacity)
    local_place = (seg_row % rows_local * blocks_local + seg_block % blocks_local).astype(
        jnp.float32
    )
    send_values = (
        jnp.zeros((devices * capacity, 128), jnp.float32).at[slot].set(seg_values, mode="drop")
    )
    send_place = (
        jnp.zeros((devices * capacity,), jnp.float32).at[slot].set(local_place, mode="drop")
    )
    place_row = jnp.pad(send_place.reshape(devices, 1, capacity), ((0, 0), (0, 0), (0, 128 - capacity)))
    send = jnp.concatenate([send_values.reshape(devices, capacity, 128), place_row], axis=1)
    got = lax.all_to_all(send, ("prow", "pcol"), 0, 0, tiled=True)
    got_values = got[:, :capacity, :].reshape(devices * capacity, 128)
    got_place = got[:, capacity, :capacity].reshape(devices * capacity)
    flat = (
        front.reshape(rows_local * blocks_local, 128)
        .at[got_place.astype(jnp.int32)]
        .add(got_values)
    )
    return flat.reshape(rows_local, cols_local)


def body(front, fill_blocks, seg_values, seg_row, seg_block, seg_live, panel_start, panel_inverse):
    rows_local, cols_local = front.shape
    blocks_local = cols_local // 128
    n_prow = lax.axis_size("prow")
    n_pcol = lax.axis_size("pcol")
    pw = panel_inverse.shape[1]
    piece_rows = rows_local // n_pcol
    r = lax.axis_index("prow")
    c = lax.axis_index("pcol")

    assembled = assemble(front, seg_values, seg_row, seg_block, seg_live, n_prow, n_pcol)

    owner = [panel_start[k] // blocks_local for k in range(PANELS)]
    offset = [panel_start[k] % blocks_local * 128 for k in range(PANELS)]
    cols = [lax.dynamic_slice_in_dim(assembled, offset[k], pw, 1) for k in range(PANELS)]

    start2 = panel_start[1] * 128
    src_row = start2 // rows_local
    x_local = lax.dynamic_slice_in_dim(cols[0], start2 % rows_local, pw, 0)
    x_mine = jnp.where((r == src_row) & (c == owner[0]), x_local, 0.0)
    x_cols = spread(x_mine, n_prow * n_pcol)

    mask_local = fill_blocks.astype(jnp.float32)
    mask_two = lax.dynamic_slice_in_dim(mask_local, offset[1] // 128, pw // 128, 1)
    mask_two = jnp.repeat(mask_two.reshape(n_pcol, piece_rows // 128, pw // 128), 128, axis=2)
    mask_two = jnp.pad(mask_two.reshape(n_pcol, 1, pw), ((0, 0), (0, 0), (0, (PANELS - 1) * pw)))
    send = jnp.concatenate(cols, axis=1).reshape(n_pcol, piece_rows, PANELS * pw)
    send = jnp.concatenate([send, mask_two], axis=1)
    recv = lax.all_to_all(send, "pcol", 0, 0, tiled=False)
    piece0 = lax.dynamic_index_in_dim(recv, owner[0], 0, keepdims=False)[:piece_rows, :pw]
    from_two = lax.dynamic_index_in_dim(recv, owner[1], 0, keepdims=False)
    piece1 = from_two[:piece_rows, pw:]
    m_piece = from_two[piece_rows:, :pw]

    left0 = dot(piece0, panel_inverse[0])
    left0_x = dot(x_cols, panel_inverse[0])
    piece1 = piece1 - dot_t(left0, left0_x) * m_piece
    left1 = dot(piece1, panel_inverse[1])
    piece = jnp.concatenate([left0, left1], axis=1)

    left_rows = gather_rows(piece, "pcol", n_pcol)

    perm = []
    for sr in range(n_prow):
        for sc in range(n_pcol):
            first = sr * rows_local + sc * piece_rows
            dc = first // cols_local
            dr = first % cols_local // piece_rows
            perm.append((sr * n_pcol + sc, dr * n_pcol + dc))
    moved = lax.ppermute(piece, ("prow", "pcol"), perm)
    left_cols = lax.all_gather(moved, "prow", axis=0, tiled=True)

    product = jnp.dot(
        left_rows, left_cols.T, precision=lax.Precision.HIGH, preferred_element_type=jnp.float32
    )
    mask_full = jnp.repeat(jnp.repeat(mask_local, 128, axis=0), 128, axis=1)
    return assembled - product * mask_full


def solution(mesh):
    placed = (
        P("prow", "pcol"),
        P("prow", "pcol"),
        P(("prow", "pcol"), None),
        P(("prow", "pcol")),
        P(("prow", "pcol")),
        P(("prow", "pcol")),
        P(),
        P(),
    )
    return jax.shard_map(
        body, mesh=mesh, in_specs=placed, out_specs=P("prow", "pcol"), check_vma=False
    )
```

```python
import jax
import jax.numpy as jnp
from jax import lax
from jax.sharding import PartitionSpec as P

PANELS = 2
HIGHEST = lax.Precision.HIGHEST


def dot(a, b):
    return jnp.dot(a, b, precision=HIGHEST, preferred_element_type=jnp.float32)


def dot_t(a, b):
    dims = (((1,), (1,)), ((), ()))
    return lax.dot_general(a, b, dims, precision=HIGHEST, preferred_element_type=jnp.float32)


def gather_rows(piece, axis, n):
    spread = jnp.broadcast_to(piece[None], (n,) + piece.shape)
    got = lax.all_to_all(spread, axis, 0, 0, tiled=False)
    return got.reshape(n * piece.shape[0], piece.shape[1])


def spread(x, total):
    for bit in range(total.bit_length() - 1):
        pairs = [(i, i ^ (1 << bit)) for i in range(total)]
        x = x + lax.ppermute(x, ("prow", "pcol"), pairs)
    return x


def assemble(front, seg_values, seg_row, seg_block, seg_live, n_prow, n_pcol):
    rows_local, cols_local = front.shape
    blocks_local = cols_local // 128
    devices = n_prow * n_pcol
    seg_count = seg_values.shape[0]
    capacity = 3 * seg_count // (2 * devices)
    target = seg_row // rows_local * n_pcol + seg_block // blocks_local
    live = jnp.arange(seg_count, dtype=jnp.int32) < seg_live[0]
    onehot = (target[:, None] == jnp.arange(devices, dtype=jnp.int32)[None, :]).astype(jnp.int32)
    earlier = jnp.cumsum(onehot, axis=0) - onehot
    rank = jnp.sum(earlier * onehot, axis=1)
    slot = jnp.where(live, target * capacity + rank, devices * capacity)
    local_place = (seg_row % rows_local * blocks_local + seg_block % blocks_local).astype(
        jnp.float32
    )
    send_values = (
        jnp.zeros((devices * capacity, 128), jnp.float32).at[slot].set(seg_values, mode="drop")
    )
    send_place = (
        jnp.zeros((devices * capacity,), jnp.float32).at[slot].set(local_place, mode="drop")
    )
    got_values = lax.all_to_all(send_values, ("prow", "pcol"), 0, 0, tiled=True)
    got_place = lax.all_to_all(send_place, ("prow", "pcol"), 0, 0, tiled=True)
    flat = (
        front.reshape(rows_local * blocks_local, 128)
        .at[got_place.astype(jnp.int32)]
        .add(got_values)
    )
    return flat.reshape(rows_local, cols_local), flat.reshape(rows_local, blocks_local, 128)


def body(front, fill_blocks, seg_values, seg_row, seg_block, seg_live, panel_start, panel_inverse):
    rows_local, cols_local = front.shape
    blocks_local = cols_local // 128
    n_prow = lax.axis_size("prow")
    n_pcol = lax.axis_size("pcol")
    pw = panel_inverse.shape[1]
    piece_rows = rows_local // n_pcol
    r = lax.axis_index("prow")
    c = lax.axis_index("pcol")

    assembled, by_block = assemble(front, seg_values, seg_row, seg_block, seg_live, n_prow, n_pcol)

    owner = [panel_start[k] // blocks_local for k in range(PANELS)]
    offset = [panel_start[k] % blocks_local * 128 for k in range(PANELS)]
    cols = [
        lax.dynamic_slice_in_dim(by_block, offset[k] // 128, pw // 128, 1).reshape(rows_local, pw)
        for k in range(PANELS)
    ]

    start2 = panel_start[1] * 128
    src_row = start2 // rows_local
    x_local = lax.dynamic_slice_in_dim(cols[0], start2 % rows_local, pw, 0)
    x_mine = jnp.where((r == src_row) & (c == owner[0]), x_local, 0.0)
    x_cols = spread(x_mine, n_prow * n_pcol)

    mask_local = fill_blocks.astype(jnp.float32)
    mask_two = lax.dynamic_slice_in_dim(mask_local, offset[1] // 128, pw // 128, 1)
    mask_two = jnp.repeat(mask_two.reshape(n_pcol, piece_rows // 128, pw // 128), 128, axis=2)
    mask_two = jnp.pad(mask_two.reshape(n_pcol, 1, pw), ((0, 0), (0, 0), (0, (PANELS - 1) * pw)))
    send = jnp.concatenate(cols, axis=1).reshape(n_pcol, piece_rows, PANELS * pw)
    send = jnp.concatenate([send, mask_two], axis=1)
    recv = lax.all_to_all(send, "pcol", 0, 0, tiled=False)
    piece0 = lax.dynamic_index_in_dim(recv, owner[0], 0, keepdims=False)[:piece_rows, :pw]
    from_two = lax.dynamic_index_in_dim(recv, owner[1], 0, keepdims=False)
    piece1 = from_two[:piece_rows, pw:]
    m_piece = from_two[piece_rows:, :pw]

    left0 = dot(piece0, panel_inverse[0])
    left0_x = dot(x_cols, panel_inverse[0])
    piece1 = piece1 - dot_t(left0, left0_x) * m_piece
    left1 = dot(piece1, panel_inverse[1])
    piece = jnp.concatenate([left0, left1], axis=1)

    left_rows = gather_rows(piece, "pcol", n_pcol)

    perm = []
    for sr in range(n_prow):
        for sc in range(n_pcol):
            first = sr * rows_local + sc * piece_rows
            dc = first // cols_local
            dr = first % cols_local // piece_rows
            perm.append((sr * n_pcol + sc, dr * n_pcol + dc))
    moved = lax.ppermute(piece, ("prow", "pcol"), perm)
    left_cols = lax.all_gather(moved, "prow", axis=0, tiled=True)

    product = jnp.dot(
        left_rows, left_cols.T, precision=lax.Precision.HIGH, preferred_element_type=jnp.float32
    )
    mask_full = jnp.repeat(jnp.repeat(mask_local, 128, axis=0), 128, axis=1)
    return assembled - product * mask_full


def solution(mesh):
    placed = (
        P("prow", "pcol"),
        P("prow", "pcol"),
        P(("prow", "pcol"), None),
        P(("prow", "pcol")),
        P(("prow", "pcol")),
        P(("prow", "pcol")),
        P(),
        P(),
    )
    return jax.shard_map(
        body, mesh=mesh, in_specs=placed, out_specs=P("prow", "pcol"), check_vma=False
    )
```

```python
import jax
import jax.numpy as jnp
from jax import lax
from jax.sharding import PartitionSpec as P

PANELS = 2
HIGHEST = lax.Precision.HIGH


def dot(a, b):
    return jnp.dot(a, b, precision=HIGHEST, preferred_element_type=jnp.float32)


def dot_t(a, b):
    dims = (((1,), (1,)), ((), ()))
    return lax.dot_general(a, b, dims, precision=HIGHEST, preferred_element_type=jnp.float32)


def gather_rows(piece, axis, n):
    spread = jnp.broadcast_to(piece[None], (n,) + piece.shape)
    got = lax.all_to_all(spread, axis, 0, 0, tiled=False)
    return got.reshape(n * piece.shape[0], piece.shape[1])


def spread(x, total):
    for bit in range(total.bit_length() - 1):
        pairs = [(i, i ^ (1 << bit)) for i in range(total)]
        x = x + lax.ppermute(x, ("prow", "pcol"), pairs)
    return x


def assemble(front, seg_values, seg_row, seg_block, seg_live, n_prow, n_pcol):
    rows_local, cols_local = front.shape
    blocks_local = cols_local // 128
    devices = n_prow * n_pcol
    seg_count = seg_values.shape[0]
    capacity = 3 * seg_count // (2 * devices)
    target = seg_row // rows_local * n_pcol + seg_block // blocks_local
    live = jnp.arange(seg_count, dtype=jnp.int32) < seg_live[0]
    onehot = (target[:, None] == jnp.arange(devices, dtype=jnp.int32)[None, :]).astype(jnp.int32)
    earlier = jnp.cumsum(onehot, axis=0) - onehot
    rank = jnp.sum(earlier * onehot, axis=1)
    slot = jnp.where(live, target * capacity + rank, devices * capacity)
    local_place = (seg_row % rows_local * blocks_local + seg_block % blocks_local).astype(
        jnp.float32
    )
    send_values = (
        jnp.zeros((devices * capacity, 128), jnp.float32).at[slot].set(seg_values, mode="drop")
    )
    send_place = (
        jnp.zeros((devices * capacity,), jnp.float32).at[slot].set(local_place, mode="drop")
    )
    got_values = lax.all_to_all(send_values, ("prow", "pcol"), 0, 0, tiled=True)
    got_place = lax.all_to_all(send_place, ("prow", "pcol"), 0, 0, tiled=True)
    flat = (
        front.reshape(rows_local * blocks_local, 128)
        .at[got_place.astype(jnp.int32)]
        .add(got_values)
    )
    return flat.reshape(rows_local, cols_local)


def body(front, fill_blocks, seg_values, seg_row, seg_block, seg_live, panel_start, panel_inverse):
    rows_local, cols_local = front.shape
    blocks_local = cols_local // 128
    n_prow = lax.axis_size("prow")
    n_pcol = lax.axis_size("pcol")
    pw = panel_inverse.shape[1]
    piece_rows = rows_local // n_pcol
    r = lax.axis_index("prow")
    c = lax.axis_index("pcol")

    assembled = assemble(front, seg_values, seg_row, seg_block, seg_live, n_prow, n_pcol)

    owner = [panel_start[k] // blocks_local for k in range(PANELS)]
    offset = [panel_start[k] % blocks_local * 128 for k in range(PANELS)]
    cols = [lax.dynamic_slice_in_dim(assembled, offset[k], pw, 1) for k in range(PANELS)]

    start2 = panel_start[1] * 128
    src_row = start2 // rows_local
    x_local = lax.dynamic_slice_in_dim(cols[0], start2 % rows_local, pw, 0)
    x_mine = jnp.where((r == src_row) & (c == owner[0]), x_local, 0.0)
    x_cols = spread(x_mine, n_prow * n_pcol)

    mask_local = fill_blocks.astype(jnp.float32)
    mask_two = lax.dynamic_slice_in_dim(mask_local, offset[1] // 128, pw // 128, 1)
    mask_two = jnp.repeat(mask_two.reshape(n_pcol, piece_rows // 128, pw // 128), 128, axis=2)
    mask_two = jnp.pad(mask_two.reshape(n_pcol, 1, pw), ((0, 0), (0, 0), (0, (PANELS - 1) * pw)))
    send = jnp.concatenate(cols, axis=1).reshape(n_pcol, piece_rows, PANELS * pw)
    send = jnp.concatenate([send, mask_two], axis=1)
    recv = lax.all_to_all(send, "pcol", 0, 0, tiled=False)
    piece0 = lax.dynamic_index_in_dim(recv, owner[0], 0, keepdims=False)[:piece_rows, :pw]
    from_two = lax.dynamic_index_in_dim(recv, owner[1], 0, keepdims=False)
    piece1 = from_two[:piece_rows, pw:]
    m_piece = from_two[piece_rows:, :pw]

    left0 = dot(piece0, panel_inverse[0])
    left0_x = dot(x_cols, panel_inverse[0])
    piece1 = piece1 - dot_t(left0, left0_x) * m_piece
    left1 = dot(piece1, panel_inverse[1])
    piece = jnp.concatenate([left0, left1], axis=1)

    left_rows = gather_rows(piece, "pcol", n_pcol)

    perm = []
    for sr in range(n_prow):
        for sc in range(n_pcol):
            first = sr * rows_local + sc * piece_rows
            dc = first // cols_local
            dr = first % cols_local // piece_rows
            perm.append((sr * n_pcol + sc, dr * n_pcol + dc))
    moved = lax.ppermute(piece, ("prow", "pcol"), perm)
    left_cols = lax.all_gather(moved, "prow", axis=0, tiled=True)

    product = jnp.dot(
        left_rows, left_cols.T, precision=lax.Precision.HIGH, preferred_element_type=jnp.float32
    )
    mask_full = jnp.repeat(jnp.repeat(mask_local, 128, axis=0), 128, axis=1)
    return assembled - product * mask_full


def solution(mesh):
    placed = (
        P("prow", "pcol"),
        P("prow", "pcol"),
        P(("prow", "pcol"), None),
        P(("prow", "pcol")),
        P(("prow", "pcol")),
        P(("prow", "pcol")),
        P(),
        P(),
    )
    return jax.shard_map(
        body, mesh=mesh, in_specs=placed, out_specs=P("prow", "pcol"), check_vma=False
    )
```

```python
import jax
import jax.numpy as jnp
from jax import lax
from jax.sharding import PartitionSpec as P

PANELS = 2
HIGHEST = lax.Precision.HIGHEST


def dot(a, b):
    return jnp.dot(a, b, precision=HIGHEST, preferred_element_type=jnp.float32)


def dot_t(a, b):
    dims = (((1,), (1,)), ((), ()))
    return lax.dot_general(a, b, dims, precision=HIGHEST, preferred_element_type=jnp.float32)


def gather_rows(piece, axis, n):
    spread = jnp.broadcast_to(piece[None], (n,) + piece.shape)
    got = lax.all_to_all(spread, axis, 0, 0, tiled=False)
    return got.reshape(n * piece.shape[0], piece.shape[1])


def spread(x, total):
    for bit in range(total.bit_length() - 1):
        pairs = [(i, i ^ (1 << bit)) for i in range(total)]
        x = x + lax.ppermute(x, ("prow", "pcol"), pairs)
    return x


def assemble(front, seg_values, seg_row, seg_block, seg_live, n_prow, n_pcol):
    rows_local, cols_local = front.shape
    blocks_local = cols_local // 128
    devices = n_prow * n_pcol
    seg_count = seg_values.shape[0]
    capacity = 3 * seg_count // (2 * devices)
    target = seg_row // rows_local * n_pcol + seg_block // blocks_local
    live = jnp.arange(seg_count, dtype=jnp.int32) < seg_live[0]
    onehot = (target[:, None] == jnp.arange(devices, dtype=jnp.int32)[None, :]).astype(jnp.int32)
    earlier = jnp.cumsum(onehot, axis=0) - onehot
    rank = jnp.sum(earlier * onehot, axis=1)
    slot = jnp.where(live, target * capacity + rank, devices * capacity)
    local_place = (seg_row % rows_local * blocks_local + seg_block % blocks_local).astype(
        jnp.float32
    )
    send_values = (
        jnp.zeros((devices * capacity, 128), jnp.float32).at[slot].set(seg_values, mode="drop")
    )
    send_place = (
        jnp.zeros((devices * capacity,), jnp.float32).at[slot].set(local_place, mode="drop")
    )
    got_values = lax.all_to_all(send_values, ("prow", "pcol"), 0, 0, tiled=True)
    got_place = lax.all_to_all(send_place, ("prow", "pcol"), 0, 0, tiled=True)
    flat = (
        front.reshape(rows_local * blocks_local, 128)
        .at[got_place.astype(jnp.int32)]
        .add(got_values)
    )
    return flat.reshape(rows_local, cols_local)


def body(front, fill_blocks, seg_values, seg_row, seg_block, seg_live, panel_start, panel_inverse):
    rows_local, cols_local = front.shape
    blocks_local = cols_local // 128
    n_prow = lax.axis_size("prow")
    n_pcol = lax.axis_size("pcol")
    pw = panel_inverse.shape[1]
    piece_rows = rows_local // n_pcol
    r = lax.axis_index("prow")
    c = lax.axis_index("pcol")

    assembled = assemble(front, seg_values, seg_row, seg_block, seg_live, n_prow, n_pcol)

    owner = [panel_start[k] // blocks_local for k in range(PANELS)]
    offset = [panel_start[k] % blocks_local * 128 for k in range(PANELS)]
    cols = [lax.dynamic_slice_in_dim(assembled, offset[k], pw, 1) for k in range(PANELS)]

    start2 = panel_start[1] * 128
    src_row = start2 // rows_local
    x_local = lax.dynamic_slice_in_dim(cols[0], start2 % rows_local, pw, 0)
    x_mine = jnp.where((r == src_row) & (c == owner[0]), x_local, 0.0)
    x_cols = spread(x_mine, n_prow * n_pcol)

    mask_local = fill_blocks.astype(jnp.float32)
    mask_two = lax.dynamic_slice_in_dim(mask_local, offset[1] // 128, pw // 128, 1)
    mask_two = jnp.repeat(mask_two.reshape(n_pcol, piece_rows // 128, pw // 128), 128, axis=2)
    recv_mask = lax.all_to_all(mask_two.reshape(n_pcol, 1, pw), "pcol", 0, 0, tiled=False)
    send = jnp.concatenate(cols, axis=1).reshape(n_pcol, piece_rows, PANELS * pw)
    recv = lax.all_to_all(send, "pcol", 0, 0, tiled=False)
    piece0 = lax.dynamic_index_in_dim(recv, owner[0], 0, keepdims=False)[:, :pw]
    piece1 = lax.dynamic_index_in_dim(recv, owner[1], 0, keepdims=False)[:, pw:]
    m_piece = lax.dynamic_index_in_dim(recv_mask, owner[1], 0, keepdims=False)

    left0 = dot(piece0, panel_inverse[0])
    left0_x = dot(x_cols, panel_inverse[0])
    piece1 = piece1 - dot_t(left0, left0_x) * m_piece
    left1 = dot(piece1, panel_inverse[1])
    piece = jnp.concatenate([left0, left1], axis=1)

    left_rows = gather_rows(piece, "pcol", n_pcol)

    perm = []
    for sr in range(n_prow):
        for sc in range(n_pcol):
            first = sr * rows_local + sc * piece_rows
            dc = first // cols_local
            dr = first % cols_local // piece_rows
            perm.append((sr * n_pcol + sc, dr * n_pcol + dc))
    moved = lax.ppermute(piece, ("prow", "pcol"), perm)
    left_cols = lax.all_gather(moved, "prow", axis=0, tiled=True)

    product = jnp.dot(
        left_rows, left_cols.T, precision=lax.Precision.HIGH, preferred_element_type=jnp.float32
    )
    mask_full = jnp.repeat(jnp.repeat(mask_local, 128, axis=0), 128, axis=1)
    return assembled - product * mask_full


def solution(mesh):
    placed = (
        P("prow", "pcol"),
        P("prow", "pcol"),
        P(("prow", "pcol"), None),
        P(("prow", "pcol")),
        P(("prow", "pcol")),
        P(("prow", "pcol")),
        P(),
        P(),
    )
    return jax.shard_map(
        body, mesh=mesh, in_specs=placed, out_specs=P("prow", "pcol"), check_vma=False
    )
```
